512 devices in a mesh: clus: 128 (over x, z, core), sub: 4 (over y).
Axes of the slice: x: 4, y: 4, z: 16, core: 2. Of those that a mesh axis runs over, the one named last changes fastest.
Arguments:
- residual_in: float32 [2048, 32, 512], P(('clus', 'sub')), may hold values from -6 to 6
- local_inverse: bfloat16 [2048, 512, 512], P(('clus', 'sub')), may hold values from -3 to 3
- coarse_basis: float32 [2048, 8, 512], P(('clus', 'sub')), may hold values from -0.6 to 0.6
- level2_inverse: float32 [128, 128, 128], P('clus'), may hold values from -3 to 3
- level2_basis: float32 [128, 32, 128], P('clus'), may hold values from -1.5 to 1.5
- level3_inverse: float32 [4096, 4096], P('clus'), may hold values from -3 to 3
Outputs:
- preconditioned: float32 [2048, 32, 512], P(('clus', 'sub'))
The draws below stay inside these ranges and needn't reach their ends.
All inputs are finite; a program needn't handle non-finite values.
Results may differ from the reference program's by a relative error of at most 0.00084.
Values sent between devices are 32-bit elements; how exact they have to be, the bound alone decides.
No kernel may reach another device: no remote copies, remote signals or barrier semaphores. Data moves between devices by JAX's collectives and lax.ppermute only.
A program may use at most 64 MiB of HBM per device.

```python
import jax
import jax.numpy as jnp
from jax import lax

NLOC = 512
IFW = 128
NRHS = 32
NC = 8
NC3 = 32
SUBS = 2048
N2 = 128
N3 = 4096
N_CLUS = 128


def dominant(key, lead, order):
    first, second = jax.random.split(jax.random.fold_in(key, 17))
    diag_values = jnp.exp(jax.random.uniform(first, (lead, order, 1), jnp.float32, -0.69, 0.69))
    spread = jax.random.normal(second, (lead, order, order), jnp.float32) * (0.5 / order ** 0.5)
    spread = jnp.clip(spread, -0.5, 0.5)
    unit = jnp.eye(order, dtype=jnp.float32)[None]
    return unit * diag_values + spread


def draw_local_inverse(key, part):
    return dominant(key, SUBS, NLOC).astype(jnp.bfloat16)


def draw_level2_inverse(key, part):
    return dominant(key, N_CLUS, N2)


def draw_level3_inverse(key, part):
    return dominant(key, 1, N3)[0]


def shard_levels(key, extent, pieces, low, high):
    loudness, own = 1.0, jax.random.fold_in(key, 6)
    for axis_at, shards_of in pieces:
        heights = jnp.exp(jax.random.uniform(jax.random.fold_in(own, axis_at), (shards_of,), jnp.float32, low / len(pieces), high / len(pieces)))
        loudness = loudness * jnp.repeat(heights, extent[axis_at] // shards_of).reshape([-1 if axis == axis_at else 1 for axis in range(len(extent))])
    return loudness


def noise(own_key, extent, deviation, limit, cuts=(), kind=jnp.bfloat16):
    result = deviation * jax.random.normal(own_key, extent, jnp.float32)
    if cuts:
        result = result * shard_levels(own_key, extent, cuts, -0.22, 0.18)
    return jnp.clip(result, -limit, limit).astype(kind)


def setup_inputs(seed: int = 0) -> dict:
    seeds = jax.random.split(jax.random.key(seed), 7)
    residual_in = noise(seeds[0], (SUBS, NRHS, NLOC), 1.0, 6.0, ((0, 512),), jnp.float32)
    local_inverse = draw_local_inverse(jax.random.fold_in(seeds[6], 71), 0)
    coarse_basis = noise(seeds[2], (SUBS, NC, NLOC), 0.1, 0.6, ((0, 512),), jnp.float32)
    level2_inverse = draw_level2_inverse(jax.random.fold_in(seeds[6], 71), 0)
    level2_basis = noise(seeds[4], (N_CLUS, NC3, N2), 0.25, 1.5, ((0, 128),), jnp.float32)
    level3_inverse = draw_level3_inverse(jax.random.fold_in(seeds[6], 71), 0)
    return dict(residual_in=residual_in, local_inverse=local_inverse, coarse_basis=coarse_basis, level2_inverse=level2_inverse, level2_basis=level2_basis, level3_inverse=level3_inverse)


def couple(values_in, rim_width):
    zero_rim = jnp.zeros_like(values_in[:1, :, :rim_width])
    from_prev = jnp.concatenate([zero_rim, values_in[:-1, :, -rim_width:]], 0)
    from_next = jnp.concatenate([values_in[1:, :, :rim_width], zero_rim], 0)
    coupled = values_in.at[:, :, :rim_width].add(0.5 * from_prev)
    return coupled.at[:, :, -rim_width:].add(0.5 * from_next)


def reference(residual_in, local_inverse, coarse_basis, level2_inverse, level2_basis, level3_inverse):
    high = lax.Precision.HIGHEST
    rhs = couple(residual_in, IFW)
    rhs_low = rhs.astype(jnp.bfloat16)

    def solve_one(pair):
        return jnp.dot(pair[1], pair[0].T, preferred_element_type=jnp.float32)

    local = lax.map(solve_one, (local_inverse, rhs_low))
    coarse = jnp.einsum("snk,srk->snr", coarse_basis, rhs, precision=high)
    groups = coarse.reshape(N_CLUS, N2, NRHS)
    level2 = jnp.einsum("cij,cjr->cir", level2_inverse, groups, precision=high)
    level3_in = jnp.einsum("cmj,cjr->cmr", level2_basis, groups, precision=high).reshape(N3, NRHS)
    level3 = jnp.dot(level3_inverse, level3_in, precision=high).reshape(N_CLUS, NC3, NRHS)
    corrected = level2 + jnp.einsum("cmj,cmr->cjr", level2_basis, level3, precision=high)
    per_sub = corrected.reshape(SUBS, NC, NRHS)
    update = local + jnp.einsum("snk,snr->srk", coarse_basis, per_sub, precision=high)
    return couple(update, IFW)
```

```python
import jax
import jax.numpy as jnp
from jax import lax
from jax.sharding import Mesh, PartitionSpec as P

IFW = 128


def from_behind_2(array, axis, by):
    count = lax.axis_size(axis)
    pairs = [(i, i + by) for i in range(count) if 0 <= i + by < count]
    return lax.ppermute(array, axis, pairs)


def couple(values_in):
    lower_rim = values_in[:, :, :IFW]
    upper_rim = values_in[:, :, values_in.shape[2] - IFW :]
    from_before = from_behind_2(upper_rim[-1:], ("x", "z", "core", "sub"), 1)
    from_behind = from_behind_2(lower_rim[:1], ("x", "z", "core", "sub"), -1)
    prev_rims = jnp.concatenate([from_before, upper_rim[:-1]], 0)
    next_rims = jnp.concatenate([lower_rim[1:], from_behind], 0)
    coupled = values_in.at[:, :, :IFW].add(0.5 * prev_rims)
    return coupled.at[:, :, values_in.shape[2] - IFW :].add(0.5 * next_rims)


def shards(residual_in, local_inverse, coarse_basis, level2_inverse, level2_basis, level3_inverse):
    high = lax.Precision.HIGHEST
    rhs = couple(residual_in)
    rhs_low = rhs.astype(jnp.bfloat16)
    local = jnp.einsum("srk,sjk->srj", rhs_low, local_inverse, preferred_element_type=jnp.float32)
    coarse = jnp.einsum("snk,srk->snr", coarse_basis, rhs, precision=high)
    gathered = lax.all_gather(coarse, "sub", axis=0, tiled=True)
    groups = gathered.reshape(-1, gathered.shape[2])
    level2 = jnp.dot(level2_inverse[0], groups, precision=high)
    level3_in = jnp.dot(level2_basis[0], groups, precision=high)
    position = lax.axis_index("sub")
    gathered_in = level3_in
    for axis in ("core", "z", "x"):
        gathered_in = lax.all_gather(gathered_in, axis, axis=0, tiled=True)
    level3 = jnp.dot(level3_inverse, gathered_in, precision=high)
    corrected = level2 + jnp.dot(level2_basis[0].T, level3, precision=high)
    own_count = coarse.shape[0] * coarse.shape[1]
    own_rows = lax.dynamic_slice_in_dim(corrected, position * own_count, own_count, 0)
    per_sub = own_rows.reshape(coarse.shape[0], coarse.shape[1], -1)
    update = local + jnp.einsum("snk,snr->srk", coarse_basis, per_sub, precision=high)
    return couple(update)


def solution(mesh):
    clus, sub = mesh.shape["clus"], mesh.shape["sub"]
    x_size = 4
    z_size = clus // (2 * x_size)
    split = Mesh(mesh.devices.reshape(x_size, z_size, 2, sub), ("x", "z", "core", "sub"))
    clus_axes = ("x", "z", "core")
    spread = (*clus_axes, "sub")
    in_specs = (
        P(spread, None, None),
        P(spread, None, None),
        P(spread, None, None),
        P(clus_axes, None, None),
        P(clus_axes, None, None),
        P(clus_axes, None),
    )
    out_specs = P(spread, None, None)
    return jax.shard_map(shards, mesh=split, in_specs=in_specs, out_specs=out_specs, check_vma=False)
```

```python
import jax
import jax.numpy as jnp
from jax import lax
from jax.sharding import Mesh, PartitionSpec as P

IFW = 128
SPREAD = ("x", "z", "core", "sub")


def from_behind_2(array, axis, by, only=None):
    count = lax.axis_size(axis)
    pairs = [(i, i + by) for i in range(count) if 0 <= i + by < count and (only is None or only(i))]
    return lax.ppermute(array, axis, pairs)


def couple(values_in):
    lower_rim = values_in[:, :, :IFW]
    upper_rim = values_in[:, :, values_in.shape[2] - IFW :]
    from_before = from_behind_2(upper_rim[-1:], SPREAD, 1)
    from_behind = from_behind_2(lower_rim[:1], SPREAD, -1)
    return add_rims(values_in, from_before, from_behind)


def add_rims(values_in, from_before, from_behind):
    lower_rim = values_in[:, :, :IFW]
    upper_rim = values_in[:, :, values_in.shape[2] - IFW :]
    prev_rims = jnp.concatenate([from_before, upper_rim[:-1]], 0)
    next_rims = jnp.concatenate([lower_rim[1:], from_behind], 0)
    coupled = values_in.at[:, :, :IFW].add(0.5 * prev_rims)
    return coupled.at[:, :, values_in.shape[2] - IFW :].add(0.5 * next_rims)


def rim_update(local_rim, basis_rim, coefficients):
    high = lax.Precision.HIGHEST
    return local_rim + jnp.einsum("snk,snr->srk", basis_rim, coefficients[None], precision=high)


def shards(residual_in, local_inverse, coarse_basis, level2_inverse, level2_basis, level3_inverse):
    high = lax.Precision.HIGHEST
    sub = lax.axis_size("sub")
    position = lax.axis_index("sub")
    nloc = residual_in.shape[2]
    nc = coarse_basis.shape[1]
    rhs = couple(residual_in)
    rhs_low = rhs.astype(jnp.bfloat16)
    local = jnp.einsum("srk,sjk->srj", rhs_low, local_inverse, preferred_element_type=jnp.float32)
    coarse = jnp.einsum("snk,srk->snr", coarse_basis, rhs, precision=high)
    nrhs = local.shape[1]

    first_local = local[0, :, :IFW]
    last_local = local[-1, :, nloc - IFW :]
    first_basis = coarse_basis[0, :, :IFW]
    last_basis = coarse_basis[-1, :, nloc - IFW :]
    sizes = [coarse.size, nrhs * IFW, nrhs * IFW, nc * IFW, nc * IFW]
    starts = [sum(sizes[:i]) for i in range(len(sizes) + 1)]
    packed = jnp.concatenate(
        [coarse.reshape(-1), first_local.reshape(-1), last_local.reshape(-1),
         first_basis.reshape(-1), last_basis.reshape(-1)], 0)
    gathered = lax.all_gather(packed, "sub", axis=0, tiled=False)
    groups = gathered[:, : starts[1]].reshape(-1, nrhs)
    level2 = jnp.dot(level2_inverse[0], groups, precision=high)
    level3_in = jnp.dot(level2_basis[0], groups, precision=high)

    is_last = position == sub - 1
    last_fold = jnp.dot(level2_basis[0][:, -nc:].T, level3_inverse, precision=high)
    first_fold = jnp.dot(level2_basis[0][:, :nc].T, level3_inverse, precision=high)
    to_last = jnp.concatenate(
        [last_local.reshape(-1), last_basis.reshape(-1), last_fold.reshape(-1), level2[-nc:].reshape(-1)], 0)
    to_first = jnp.concatenate(
        [first_local.reshape(-1), first_basis.reshape(-1), first_fold.reshape(-1), level2[:nc].reshape(-1)], 0)
    outgoing = jnp.where(is_last, to_last, to_first)
    count = lax.axis_size(SPREAD)
    pairs = [(i, i + 1) for i in range(sub - 1, count - 1, sub)] + [(i + 1, i) for i in range(sub - 1, count - 1, sub)]
    incoming = lax.ppermute(outgoing, SPREAD, pairs)

    gathered_in = level3_in
    for axis in ("core", "z", "x"):
        gathered_in = lax.all_gather(gathered_in, axis, axis=0, tiled=True)
    level3 = jnp.dot(level3_inverse, gathered_in, precision=high)
    corrected = level2 + jnp.dot(level2_basis[0].T, level3, precision=high)
    own_count = coarse.shape[0] * coarse.shape[1]
    own_rows = lax.dynamic_slice_in_dim(corrected, position * own_count, own_count, 0)
    per_sub = own_rows.reshape(coarse.shape[0], coarse.shape[1], -1)
    update = local + jnp.einsum("snk,snr->srk", coarse_basis, per_sub, precision=high)

    cut = [nrhs * IFW, nc * IFW, nc * level3_inverse.shape[1], nc * nrhs]
    at = [sum(cut[:i]) for i in range(len(cut) + 1)]
    cross_local = incoming[at[0] : at[1]].reshape(1, nrhs, IFW)
    cross_basis = incoming[at[1] : at[2]].reshape(1, nc, IFW)
    cross_fold = incoming[at[2] : at[3]].reshape(nc, -1)
    cross_rows = incoming[at[3] : at[4]].reshape(nc, nrhs)
    cross_coef = cross_rows + jnp.dot(cross_fold, gathered_in, precision=high)
    cross_rim = rim_update(cross_local, cross_basis, cross_coef)

    prev_device = lax.dynamic_index_in_dim(gathered, jnp.maximum(position - 1, 0), 0, keepdims=False)
    next_device = lax.dynamic_index_in_dim(gathered, jnp.minimum(position + 1, sub - 1), 0, keepdims=False)
    prev_rows = lax.dynamic_slice_in_dim(corrected, position * own_count - nc, nc, 0)
    next_rows = lax.dynamic_slice_in_dim(corrected, (position + 1) * own_count, nc, 0)
    inner_before = rim_update(
        prev_device[starts[2] : starts[3]].reshape(1, nrhs, IFW),
        prev_device[starts[4] : starts[5]].reshape(1, nc, IFW), prev_rows)
    inner_behind = rim_update(
        next_device[starts[1] : starts[2]].reshape(1, nrhs, IFW),
        next_device[starts[3] : starts[4]].reshape(1, nc, IFW), next_rows)
    from_before = jnp.where(position > 0, inner_before, cross_rim)
    from_behind = jnp.where(is_last, cross_rim, inner_behind)
    return add_rims(update, from_before, from_behind)


def solution(mesh):
    clus, sub = mesh.shape["clus"], mesh.shape["sub"]
    x_size = 4
    z_size = clus // (2 * x_size)
    split = Mesh(mesh.devices.reshape(x_size, z_size, 2, sub), SPREAD)
    clus_axes = ("x", "z", "core")
    in_specs = (
        P(SPREAD, None, None),
        P(SPREAD, None, None),
        P(SPREAD, None, None),
        P(clus_axes, None, None),
        P(clus_axes, None, None),
        P(clus_axes, None),
    )
    out_specs = P(SPREAD, None, None)
    return jax.shard_map(shards, mesh=split, in_specs=in_specs, out_specs=out_specs, check_vma=False)
```

```python
import jax
import jax.numpy as jnp
from jax import lax
from jax.sharding import Mesh, PartitionSpec as P

IFW = 128
SPREAD = ("x", "z", "core", "sub")


def from_behind_2(array, axis, by, only=None):
    count = lax.axis_size(axis)
    pairs = [(i, i + by) for i in range(count) if 0 <= i + by < count and (only is None or only(i))]
    return lax.ppermute(array, axis, pairs)


def couple(values_in):
    lower_rim = values_in[:, :, :IFW]
    upper_rim = values_in[:, :, values_in.shape[2] - IFW :]
    from_before = from_behind_2(upper_rim[-1:], SPREAD, 1)
    from_behind = from_behind_2(lower_rim[:1], SPREAD, -1)
    return add_rims(values_in, from_before, from_behind)


def add_rims(values_in, from_before, from_behind):
    lower_rim = values_in[:, :, :IFW]
    upper_rim = values_in[:, :, values_in.shape[2] - IFW :]
    prev_rims = jnp.concatenate([from_before, upper_rim[:-1]], 0)
    next_rims = jnp.concatenate([lower_rim[1:], from_behind], 0)
    coupled = values_in.at[:, :, :IFW].add(0.5 * prev_rims)
    return coupled.at[:, :, values_in.shape[2] - IFW :].add(0.5 * next_rims)


def rim_update(local_rim, basis_rim, coefficients):
    high = lax.Precision.HIGHEST
    return local_rim + jnp.einsum("snk,snr->srk", basis_rim, coefficients[None], precision=high)


def shards(residual_in, local_inverse, coarse_basis, level2_inverse, level2_basis, level3_inverse):
    high = lax.Precision.HIGHEST
    sub = lax.axis_size("sub")
    position = lax.axis_index("sub")
    nloc = residual_in.shape[2]
    nc = coarse_basis.shape[1]
    rhs = couple(residual_in)
    rhs_low = rhs.astype(jnp.bfloat16)
    local = jnp.einsum("srk,sjk->srj", rhs_low, local_inverse, preferred_element_type=jnp.float32)
    coarse = jnp.einsum("snk,srk->snr", coarse_basis, rhs, precision=high)
    nrhs = local.shape[1]

    first_local = local[0, :, :IFW]
    last_local = local[-1, :, nloc - IFW :]
    first_basis = coarse_basis[0, :, :IFW]
    last_basis = coarse_basis[-1, :, nloc - IFW :]
    coarse_rows = coarse.size // IFW
    rows = [coarse_rows, nrhs, nrhs, nc, nc]
    at = [sum(rows[:i]) for i in range(len(rows) + 1)]
    packed = jnp.concatenate(
        [coarse.reshape(coarse_rows, IFW), first_local, last_local, first_basis, last_basis], 0)
    gathered = lax.all_gather(packed, "sub", axis=0, tiled=False)
    groups = gathered[:, : at[1]].reshape(-1, nrhs)
    level2 = jnp.dot(level2_inverse[0], groups, precision=high)
    level3_in = jnp.dot(level2_basis[0], groups, precision=high)

    is_last = position == sub - 1
    n3 = level3_inverse.shape[1]
    pick = jnp.where(is_last, level2_basis[0][:, -nc:], level2_basis[0][:, :nc])
    fold = jnp.dot(pick.T, level3_inverse, precision=high)
    edge_rows = jnp.where(is_last, level2[-nc:], level2[:nc])
    edge_local = jnp.where(is_last, last_local, first_local)
    edge_basis = jnp.where(is_last, last_basis, first_basis)
    cut = [nrhs, nc, nc * n3 // IFW, nc * nrhs // IFW]
    on = [sum(cut[:i]) for i in range(len(cut) + 1)]
    outgoing = jnp.concatenate(
        [edge_local, edge_basis, fold.reshape(-1, IFW), edge_rows.reshape(-1, IFW)], 0)
    count = lax.axis_size(SPREAD)
    pairs = [(i, i + 1) for i in range(sub - 1, count - 1, sub)] + [(i + 1, i) for i in range(sub - 1, count - 1, sub)]
    incoming = lax.ppermute(outgoing, SPREAD, pairs)

    gathered_in = level3_in
    for axis in ("core", "z", "x"):
        gathered_in = lax.all_gather(gathered_in, axis, axis=0, tiled=True)
    level3 = jnp.dot(level3_inverse, gathered_in, precision=high)
    corrected = level2 + jnp.dot(level2_basis[0].T, level3, precision=high)
    own_count = coarse.shape[0] * coarse.shape[1]
    own_rows = lax.dynamic_slice_in_dim(corrected, position * own_count, own_count, 0)
    per_sub = own_rows.reshape(coarse.shape[0], coarse.shape[1], -1)
    update = local + jnp.einsum("snk,snr->srk", coarse_basis, per_sub, precision=high)

    cross_fold = incoming[on[2] : on[3]].reshape(nc, n3)
    cross_rows = incoming[on[3] : on[4]].reshape(nc, nrhs)
    cross_coef = cross_rows + jnp.dot(cross_fold, gathered_in, precision=high)

    prev_device = lax.dynamic_index_in_dim(gathered, jnp.maximum(position - 1, 0), 0, keepdims=False)
    next_device = lax.dynamic_index_in_dim(gathered, jnp.minimum(position + 1, sub - 1), 0, keepdims=False)
    prev_rows = lax.dynamic_slice_in_dim(corrected, position * own_count - nc, nc, 0)
    next_rows = lax.dynamic_slice_in_dim(corrected, (position + 1) * own_count, nc, 0)
    first = position == 0
    before_local = jnp.where(first, incoming[on[0] : on[1]], prev_device[at[2] : at[3]])
    before_basis = jnp.where(first, incoming[on[1] : on[2]], prev_device[at[4] : at[5]])
    before_coef = jnp.where(first, cross_coef, prev_rows)
    behind_local = jnp.where(is_last, incoming[on[0] : on[1]], next_device[at[1] : at[2]])
    behind_basis = jnp.where(is_last, incoming[on[1] : on[2]], next_device[at[3] : at[4]])
    behind_coef = jnp.where(is_last, cross_coef, next_rows)
    from_before = rim_update(before_local[None], before_basis[None], before_coef)
    from_behind = rim_update(behind_local[None], behind_basis[None], behind_coef)
    return add_rims(update, from_before, from_behind)


def solution(mesh):
    clus, sub = mesh.shape["clus"], mesh.shape["sub"]
    x_size = 4
    z_size = clus // (2 * x_size)
    split = Mesh(mesh.devices.reshape(x_size, z_size, 2, sub), SPREAD)
    clus_axes = ("x", "z", "core")
    in_specs = (
        P(SPREAD, None, None),
        P(SPREAD, None, None),
        P(SPREAD, None, None),
        P(clus_axes, None, None),
        P(clus_axes, None, None),
        P(clus_axes, None),
    )
    out_specs = P(SPREAD, None, None)
    return jax.shard_map(shards, mesh=split, in_specs=in_specs, out_specs=out_specs, check_vma=False)
```

```python
import jax
import jax.numpy as jnp
from jax import lax
from jax.sharding import Mesh, PartitionSpec as P

IFW = 128
SPREAD = ("x", "z", "core", "sub")


def from_behind_2(array, axis, by, only=None):
    count = lax.axis_size(axis)
    pairs = [(i, i + by) for i in range(count) if 0 <= i + by < count and (only is None or only(i))]
    return lax.ppermute(array, axis, pairs)


def couple(values_in):
    lower_rim = values_in[:, :, :IFW]
    upper_rim = values_in[:, :, values_in.shape[2] - IFW :]
    from_before = from_behind_2(upper_rim[-1:], SPREAD, 1)
    from_behind = from_behind_2(lower_rim[:1], SPREAD, -1)
    return add_rims(values_in, from_before, from_behind)


def add_rims(values_in, from_before, from_behind):
    lower_rim = values_in[:, :, :IFW]
    upper_rim = values_in[:, :, values_in.shape[2] - IFW :]
    prev_rims = jnp.concatenate([from_before, upper_rim[:-1]], 0)
    next_rims = jnp.concatenate([lower_rim[1:], from_behind], 0)
    coupled = values_in.at[:, :, :IFW].add(0.5 * prev_rims)
    return coupled.at[:, :, values_in.shape[2] - IFW :].add(0.5 * next_rims)


def rim_update(local_rim, basis_rim, coefficients):
    high = lax.Precision.HIGHEST
    return local_rim + jnp.einsum("snk,snr->srk", basis_rim, coefficients[None], precision=high)


def shards(residual_in, local_inverse, coarse_basis, level2_inverse, level2_basis, level3_inverse):
    high = lax.Precision.HIGHEST
    sub = lax.axis_size("sub")
    position = lax.axis_index("sub")
    nloc = residual_in.shape[2]
    nc = coarse_basis.shape[1]
    rhs = couple(residual_in)
    rhs_low = rhs.astype(jnp.bfloat16)
    local = jnp.einsum("srk,sjk->srj", rhs_low, local_inverse, preferred_element_type=jnp.float32)
    coarse = jnp.einsum("snk,srk->snr", coarse_basis, rhs, precision=high)
    nrhs = local.shape[1]

    first_local = local[0, :, :IFW]
    last_local = local[-1, :, nloc - IFW :]
    first_basis = coarse_basis[0, :, :IFW]
    last_basis = coarse_basis[-1, :, nloc - IFW :]
    coarse_rows = coarse.size // IFW
    rows = [coarse_rows, nrhs, nrhs, nc, nc]
    at = [sum(rows[:i]) for i in range(len(rows) + 1)]
    packed = jnp.concatenate(
        [coarse.reshape(coarse_rows, IFW), first_local, last_local, first_basis, last_basis], 0)
    gathered = lax.all_gather(packed, "sub", axis=0, tiled=False)
    groups = gathered[:, : at[1]].reshape(-1, nrhs)
    level2 = jnp.dot(level2_inverse[0], groups, precision=high)
    level3_in = jnp.dot(level2_basis[0], groups, precision=high)

    is_last = position == sub - 1
    n3 = level3_inverse.shape[1]
    pick = jnp.where(is_last, level2_basis[0][:, -nc:], level2_basis[0][:, :nc])
    fold = jnp.dot(pick.T, level3_inverse, precision=high)
    edge_rows = jnp.where(is_last, level2[-nc:], level2[:nc])
    edge_local = jnp.where(is_last, last_local, first_local)
    edge_basis = jnp.where(is_last, last_basis, first_basis)
    fold_rows = nc * n3 // IFW
    cut = [fold_rows, nrhs, nc, nc]
    on = [sum(cut[:i]) for i in range(len(cut) + 1)]
    outgoing = jnp.concatenate(
        [fold.reshape(fold_rows, IFW), edge_local, edge_basis, jnp.pad(edge_rows, ((0, 0), (0, IFW - nrhs)))], 0)
    count = lax.axis_size(SPREAD)
    pairs = [(i, i + 1) for i in range(sub - 1, count - 1, sub)] + [(i + 1, i) for i in range(sub - 1, count - 1, sub)]
    incoming = lax.ppermute(outgoing, SPREAD, pairs)

    gathered_in = level3_in
    for axis in ("core", "z", "x"):
        gathered_in = lax.all_gather(gathered_in, axis, axis=0, tiled=True)
    level3 = jnp.dot(level3_inverse, gathered_in, precision=high)
    corrected = level2 + jnp.dot(level2_basis[0].T, level3, precision=high)
    own_count = coarse.shape[0] * coarse.shape[1]
    own_rows = lax.dynamic_slice_in_dim(corrected, position * own_count, own_count, 0)
    per_sub = own_rows.reshape(coarse.shape[0], coarse.shape[1], -1)
    update = local + jnp.einsum("snk,snr->srk", coarse_basis, per_sub, precision=high)

    cross_fold = incoming[: on[1]].reshape(nc, n3)
    cross_rows = incoming[on[3] : on[4], :nrhs]
    cross_coef = cross_rows + jnp.dot(cross_fold, gathered_in, precision=high)

    prev_device = lax.dynamic_index_in_dim(gathered, jnp.maximum(position - 1, 0), 0, keepdims=False)
    next_device = lax.dynamic_index_in_dim(gathered, jnp.minimum(position + 1, sub - 1), 0, keepdims=False)
    prev_rows = lax.dynamic_slice_in_dim(corrected, position * own_count - nc, nc, 0)
    next_rows = lax.dynamic_slice_in_dim(corrected, (position + 1) * own_count, nc, 0)
    first = position == 0
    cross_local = incoming[on[1] : on[2]]
    cross_basis = incoming[on[2] : on[3]]
    rim_local = jnp.stack([
        jnp.where(first, cross_local, prev_device[at[2] : at[3]]),
        jnp.where(is_last, cross_local, next_device[at[1] : at[2]])])
    rim_basis = jnp.stack([
        jnp.where(first, cross_basis, prev_device[at[4] : at[5]]),
        jnp.where(is_last, cross_basis, next_device[at[3] : at[4]])])
    rim_coef = jnp.stack([
        jnp.where(first, cross_coef, prev_rows),
        jnp.where(is_last, cross_coef, next_rows)])
    rims = rim_local + jnp.sum(rim_basis[:, :, None, :] * rim_coef[:, :, :, None], axis=1)
    from_before = rims[0:1]
    from_behind = rims[1:2]
    return add_rims(update, from_before, from_behind)


def solution(mesh):
    clus, sub = mesh.shape["clus"], mesh.shape["sub"]
    x_size = 4
    z_size = clus // (2 * x_size)
    split = Mesh(mesh.devices.reshape(x_size, z_size, 2, sub), SPREAD)
    clus_axes = ("x", "z", "core")
    in_specs = (
        P(SPREAD, None, None),
        P(SPREAD, None, None),
        P(SPREAD, None, None),
        P(clus_axes, None, None),
        P(clus_axes, None, None),
        P(clus_axes, None),
    )
    out_specs = P(SPREAD, None, None)
    return jax.shard_map(shards, mesh=split, in_specs=in_specs, out_specs=out_specs, check_vma=False)
```

```python
import jax
import jax.numpy as jnp
from jax import lax
from jax.sharding import Mesh, PartitionSpec as P

IFW = 128
SPREAD = ("x", "z", "core", "sub")


def from_behind_2(array, axis, by, only=None):
    count = lax.axis_size(axis)
    pairs = [(i, i + by) for i in range(count) if 0 <= i + by < count and (only is None or only(i))]
    return lax.ppermute(array, axis, pairs)


def couple(values_in):
    lower_rim = values_in[:, :, :IFW]
    upper_rim = values_in[:, :, values_in.shape[2] - IFW :]
    from_before = from_behind_2(upper_rim[-1:], SPREAD, 1)
    from_behind = from_behind_2(lower_rim[:1], SPREAD, -1)
    return add_rims(values_in, from_before, from_behind)


def add_rims(values_in, from_before, from_behind):
    lower_rim = values_in[:, :, :IFW]
    upper_rim = values_in[:, :, values_in.shape[2] - IFW :]
    prev_rims = jnp.concatenate([from_before, upper_rim[:-1]], 0)
    next_rims = jnp.concatenate([lower_rim[1:], from_behind], 0)
    coupled = values_in.at[:, :, :IFW].add(0.5 * prev_rims)
    return coupled.at[:, :, values_in.shape[2] - IFW :].add(0.5 * next_rims)


def rim_update(local_rim, basis_rim, coefficients):
    high = lax.Precision.HIGHEST
    return local_rim + jnp.einsum("snk,snr->srk", basis_rim, coefficients[None], precision=high)


def shards(residual_in, local_inverse, coarse_basis, level2_inverse, level2_basis, level3_inverse):
    high = lax.Precision.HIGHEST
    sub = lax.axis_size("sub")
    position = lax.axis_index("sub")
    nloc = residual_in.shape[2]
    nc = coarse_basis.shape[1]
    rhs = couple(residual_in)
    rhs_low = rhs.astype(jnp.bfloat16)
    local = jnp.einsum("srk,sjk->srj", rhs_low, local_inverse, preferred_element_type=jnp.float32)
    coarse = jnp.einsum("snk,srk->snr", coarse_basis, rhs, precision=high)
    nrhs = local.shape[1]

    first_local = local[0, :, :IFW]
    last_local = local[-1, :, nloc - IFW :]
    first_basis = coarse_basis[0, :, :IFW]
    last_basis = coarse_basis[-1, :, nloc - IFW :]
    coarse_rows = coarse.size // IFW
    rows = [coarse_rows, nrhs, nrhs, nc, nc]
    at = [sum(rows[:i]) for i in range(len(rows) + 1)]
    packed = jnp.concatenate(
        [coarse.reshape(coarse_rows, IFW), first_local, last_local, first_basis, last_basis], 0)
    gathered = lax.all_gather(packed, "sub", axis=0, tiled=False)
    groups = gathered[:, : at[1]].reshape(-1, nrhs)
    level2 = jnp.dot(level2_inverse[0], groups, precision=high)
    level3_in = jnp.dot(level2_basis[0], groups, precision=high)
    level2, level3_in = lax.optimization_barrier((level2, level3_in))

    is_last = position == sub - 1
    n3 = level3_inverse.shape[1]
    pick = jnp.where(is_last, level2_basis[0][:, -nc:], level2_basis[0][:, :nc])
    fold = jnp.dot(pick.T, level3_inverse, precision=high)
    edge_rows = jnp.where(is_last, level2[-nc:], level2[:nc])
    edge_local = jnp.where(is_last, last_local, first_local)
    edge_basis = jnp.where(is_last, last_basis, first_basis)
    fold_rows = nc * n3 // IFW
    cut = [fold_rows, nrhs, nc, nc]
    on = [sum(cut[:i]) for i in range(len(cut) + 1)]
    outgoing = jnp.concatenate(
        [fold.reshape(fold_rows, IFW), edge_local, edge_basis, jnp.pad(edge_rows, ((0, 0), (0, IFW - nrhs)))], 0)
    count = lax.axis_size(SPREAD)
    pairs = [(i, i + 1) for i in range(sub - 1, count - 1, sub)] + [(i + 1, i) for i in range(sub - 1, count - 1, sub)]
    incoming = lax.ppermute(outgoing, SPREAD, pairs)

    gathered_in = level3_in
    for axis in ("core", "z", "x"):
        gathered_in = lax.all_gather(gathered_in, axis, axis=0, tiled=True)
    incoming, gathered_in = lax.optimization_barrier((incoming, gathered_in))
    level3 = jnp.dot(level3_inverse, gathered_in, precision=high)
    corrected = level2 + jnp.dot(level2_basis[0].T, level3, precision=high)
    own_count = coarse.shape[0] * coarse.shape[1]
    own_rows = lax.dynamic_slice_in_dim(corrected, position * own_count, own_count, 0)
    per_sub = own_rows.reshape(coarse.shape[0], coarse.shape[1], -1)

    cross_fold = incoming[: on[1]].reshape(nc, n3)
    cross_rows = incoming[on[3] : on[4], :nrhs]
    cross_coef = cross_rows + jnp.dot(cross_fold, gathered_in, precision=high)

    prev_device = lax.dynamic_index_in_dim(gathered, jnp.maximum(position - 1, 0), 0, keepdims=False)
    next_device = lax.dynamic_index_in_dim(gathered, jnp.minimum(position + 1, sub - 1), 0, keepdims=False)
    prev_rows = lax.dynamic_slice_in_dim(corrected, position * own_count - nc, nc, 0)
    next_rows = lax.dynamic_slice_in_dim(corrected, (position + 1) * own_count, nc, 0)
    first = position == 0
    cross_local = incoming[on[1] : on[2]]
    cross_basis = incoming[on[2] : on[3]]
    rim_local = jnp.stack([
        jnp.where(first, cross_local, prev_device[at[2] : at[3]]),
        jnp.where(is_last, cross_local, next_device[at[1] : at[2]])])
    rim_basis = jnp.stack([
        jnp.where(first, cross_basis, prev_device[at[4] : at[5]]),
        jnp.where(is_last, cross_basis, next_device[at[3] : at[4]])])
    rim_coef = jnp.stack([
        jnp.where(first, cross_coef, prev_rows),
        jnp.where(is_last, cross_coef, next_rows)])
    rims = rim_local + jnp.sum(rim_basis[:, :, None, :] * rim_coef[:, :, :, None], axis=1)
    from_before = rims[0:1]
    from_behind = rims[1:2]
    lower = local[:, :, :IFW] + jnp.einsum("snk,snr->srk", coarse_basis[:, :, :IFW], per_sub, precision=high)
    upper = local[:, :, nloc - IFW :] + jnp.einsum(
        "snk,snr->srk", coarse_basis[:, :, nloc - IFW :], per_sub, precision=high)
    prev_rims = jnp.concatenate([from_before, upper[:-1]], 0)
    next_rims = jnp.concatenate([lower[1:], from_behind], 0)
    middle = jnp.zeros((local.shape[0], nrhs, nloc - 2 * IFW), jnp.float32)
    rim_terms = jnp.concatenate([0.5 * prev_rims, middle, 0.5 * next_rims], 2)
    update = local + jnp.einsum("snk,snr->srk", coarse_basis, per_sub, precision=high)
    return update + rim_terms


def solution(mesh):
    clus, sub = mesh.shape["clus"], mesh.shape["sub"]
    x_size = 4
    z_size = clus // (2 * x_size)
    split = Mesh(mesh.devices.reshape(x_size, z_size, 2, sub), SPREAD)
    clus_axes = ("x", "z", "core")
    in_specs = (
        P(SPREAD, None, None),
        P(SPREAD, None, None),
        P(SPREAD, None, None),
        P(clus_axes, None, None),
        P(clus_axes, None, None),
        P(clus_axes, None),
    )
    out_specs = P(SPREAD, None, None)
    return jax.shard_map(shards, mesh=split, in_specs=in_specs, out_specs=out_specs, check_vma=False)
```

```python
import jax
import jax.numpy as jnp
from jax import lax
from jax.sharding import Mesh, PartitionSpec as P

IFW = 128
SPREAD = ("x", "z", "core", "sub")


def from_behind_2(array, axis, by, only=None):
    count = lax.axis_size(axis)
    pairs = [(i, i + by) for i in range(count) if 0 <= i + by < count and (only is None or only(i))]
    return lax.ppermute(array, axis, pairs)


def couple(values_in):
    lower_rim = values_in[:, :, :IFW]
    upper_rim = values_in[:, :, values_in.shape[2] - IFW :]
    from_before = from_behind_2(upper_rim[-1:], SPREAD, 1)
    from_behind = from_behind_2(lower_rim[:1], SPREAD, -1)
    return add_rims(values_in, from_before, from_behind)


def add_rims(values_in, from_before, from_behind):
    lower_rim = values_in[:, :, :IFW]
    upper_rim = values_in[:, :, values_in.shape[2] - IFW :]
    prev_rims = jnp.concatenate([from_before, upper_rim[:-1]], 0)
    next_rims = jnp.concatenate([lower_rim[1:], from_behind], 0)
    coupled = values_in.at[:, :, :IFW].add(0.5 * prev_rims)
    return coupled.at[:, :, values_in.shape[2] - IFW :].add(0.5 * next_rims)


def rim_update(local_rim, basis_rim, coefficients):
    high = lax.Precision.HIGH
    return local_rim + jnp.einsum("snk,snr->srk", basis_rim, coefficients[None], precision=high)


def shards(residual_in, local_inverse, coarse_basis, level2_inverse, level2_basis, level3_inverse):
    high = lax.Precision.HIGH
    sub = lax.axis_size("sub")
    position = lax.axis_index("sub")
    nloc = residual_in.shape[2]
    nc = coarse_basis.shape[1]
    rhs = couple(residual_in)
    rhs_low = rhs.astype(jnp.bfloat16)
    local = jnp.einsum("srk,sjk->srj", rhs_low, local_inverse, preferred_element_type=jnp.float32)
    coarse = jnp.einsum("snk,srk->snr", coarse_basis, rhs, precision=high)
    nrhs = local.shape[1]

    first_local = local[0, :, :IFW]
    last_local = local[-1, :, nloc - IFW :]
    first_basis = coarse_basis[0, :, :IFW]
    last_basis = coarse_basis[-1, :, nloc - IFW :]
    coarse_rows = coarse.size // IFW
    rows = [coarse_rows, nrhs, nrhs, nc, nc]
    at = [sum(rows[:i]) for i in range(len(rows) + 1)]
    packed = jnp.concatenate(
        [coarse.reshape(coarse_rows, IFW), first_local, last_local, first_basis, last_basis], 0)
    gathered = lax.all_gather(packed, "sub", axis=0, tiled=False)
    groups = gathered[:, : at[1]].reshape(-1, nrhs)
    level2 = jnp.dot(level2_inverse[0], groups, precision=high)
    level3_in = jnp.dot(level2_basis[0], groups, precision=high)

    is_last = position == sub - 1
    n3 = level3_inverse.shape[1]
    pick = jnp.where(is_last, level2_basis[0][:, -nc:], level2_basis[0][:, :nc])
    fold = jnp.dot(pick.T, level3_inverse, precision=high)
    edge_rows = jnp.where(is_last, level2[-nc:], level2[:nc])
    edge_local = jnp.where(is_last, last_local, first_local)
    edge_basis = jnp.where(is_last, last_basis, first_basis)
    fold_rows = nc * n3 // IFW
    cut = [fold_rows, nrhs, nc, nc]
    on = [sum(cut[:i]) for i in range(len(cut) + 1)]
    outgoing = jnp.concatenate(
        [fold.reshape(fold_rows, IFW), edge_local, edge_basis, jnp.pad(edge_rows, ((0, 0), (0, IFW - nrhs)))], 0)
    count = lax.axis_size(SPREAD)
    pairs = [(i, i + 1) for i in range(sub - 1, count - 1, sub)] + [(i + 1, i) for i in range(sub - 1, count - 1, sub)]
    incoming = lax.ppermute(outgoing, SPREAD, pairs)

    gathered_in = level3_in
    for axis in ("core", "z", "x"):
        gathered_in = lax.all_gather(gathered_in, axis, axis=0, tiled=True)
    level3 = jnp.dot(level3_inverse, gathered_in, precision=high)
    corrected = level2 + jnp.dot(level2_basis[0].T, level3, precision=high)
    own_count = coarse.shape[0] * coarse.shape[1]
    own_rows = lax.dynamic_slice_in_dim(corrected, position * own_count, own_count, 0)
    per_sub = own_rows.reshape(coarse.shape[0], coarse.shape[1], -1)
    update = local + jnp.einsum("snk,snr->srk", coarse_basis, per_sub, precision=high)

    cross_fold = incoming[: on[1]].reshape(nc, n3)
    cross_rows = incoming[on[3] : on[4], :nrhs]
    cross_coef = cross_rows + jnp.dot(cross_fold, gathered_in, precision=high)

    prev_device = lax.dynamic_index_in_dim(gathered, jnp.maximum(position - 1, 0), 0, keepdims=False)
    next_device = lax.dynamic_index_in_dim(gathered, jnp.minimum(position + 1, sub - 1), 0, keepdims=False)
    prev_rows = lax.dynamic_slice_in_dim(corrected, position * own_count - nc, nc, 0)
    next_rows = lax.dynamic_slice_in_dim(corrected, (position + 1) * own_count, nc, 0)
    first = position == 0
    cross_local = incoming[on[1] : on[2]]
    cross_basis = incoming[on[2] : on[3]]
    rim_local = jnp.stack([
        jnp.where(first, cross_local, prev_device[at[2] : at[3]]),
        jnp.where(is_last, cross_local, next_device[at[1] : at[2]])])
    rim_basis = jnp.stack([
        jnp.where(first, cross_basis, prev_device[at[4] : at[5]]),
        jnp.where(is_last, cross_basis, next_device[at[3] : at[4]])])
    rim_coef = jnp.stack([
        jnp.where(first, cross_coef, prev_rows),
        jnp.where(is_last, cross_coef, next_rows)])
    rims = rim_local + jnp.sum(rim_basis[:, :, None, :] * rim_coef[:, :, :, None], axis=1)
    from_before = rims[0:1]
    from_behind = rims[1:2]
    return add_rims(update, from_before, from_behind)


def solution(mesh):
    clus, sub = mesh.shape["clus"], mesh.shape["sub"]
    x_size = 4
    z_size = clus // (2 * x_size)
    split = Mesh(mesh.devices.reshape(x_size, z_size, 2, sub), SPREAD)
    clus_axes = ("x", "z", "core")
    in_specs = (
        P(SPREAD, None, None),
        P(SPREAD, None, None),
        P(SPREAD, None, None),
        P(clus_axes, None, None),
        P(clus_axes, None, None),
        P(clus_axes, None),
    )
    out_specs = P(SPREAD, None, None)
    return jax.shard_map(shards, mesh=split, in_specs=in_specs, out_specs=out_specs, check_vma=False)
```

```python
import jax
import jax.numpy as jnp
from jax import lax
from jax.sharding import Mesh, PartitionSpec as P

IFW = 128
SPREAD = ("x", "z", "core", "sub")


def from_behind_2(array, axis, by, only=None):
    count = lax.axis_size(axis)
    pairs = [(i, i + by) for i in range(count) if 0 <= i + by < count and (only is None or only(i))]
    return lax.ppermute(array, axis, pairs)


def couple(values_in):
    lower_rim = values_in[:, :, :IFW]
    upper_rim = values_in[:, :, values_in.shape[2] - IFW :]
    from_before = from_behind_2(upper_rim[-1:], SPREAD, 1)
    from_behind = from_behind_2(lower_rim[:1], SPREAD, -1)
    return add_rims(values_in, from_before, from_behind)


def add_rims(values_in, from_before, from_behind):
    lower_rim = values_in[:, :, :IFW]
    upper_rim = values_in[:, :, values_in.shape[2] - IFW :]
    prev_rims = jnp.concatenate([from_before, upper_rim[:-1]], 0)
    next_rims = jnp.concatenate([lower_rim[1:], from_behind], 0)
    coupled = values_in.at[:, :, :IFW].add(0.5 * prev_rims)
    return coupled.at[:, :, values_in.shape[2] - IFW :].add(0.5 * next_rims)


def rim_update(local_rim, basis_rim, coefficients):
    high = lax.Precision.HIGH
    return local_rim + jnp.einsum("snk,snr->srk", basis_rim, coefficients[None], precision=high)


def shards(residual_in, local_inverse, coarse_basis, level2_inverse, level2_basis, level3_inverse):
    high = lax.Precision.HIGH
    sub = lax.axis_size("sub")
    position = lax.axis_index("sub")
    nloc = residual_in.shape[2]
    nc = coarse_basis.shape[1]
    rhs = couple(residual_in)
    rhs_low = rhs.astype(jnp.bfloat16)
    inner = residual_in[1:-1]
    inner = inner.at[:, :, :IFW].add(0.5 * residual_in[:-2, :, nloc - IFW :])
    inner = inner.at[:, :, nloc - IFW :].add(0.5 * residual_in[2:, :, :IFW])
    inner_local = jnp.einsum(
        "srk,sjk->srj", inner.astype(jnp.bfloat16), local_inverse[1:-1], preferred_element_type=jnp.float32)
    edge_local = jnp.einsum(
        "srk,sjk->srj", rhs_low[::residual_in.shape[0] - 1], local_inverse[::residual_in.shape[0] - 1],
        preferred_element_type=jnp.float32)
    local = jnp.concatenate([edge_local[:1], inner_local, edge_local[1:]], 0)
    coarse = jnp.einsum("snk,srk->snr", coarse_basis, rhs, precision=high)
    nrhs = local.shape[1]

    first_local = local[0, :, :IFW]
    last_local = local[-1, :, nloc - IFW :]
    first_basis = coarse_basis[0, :, :IFW]
    last_basis = coarse_basis[-1, :, nloc - IFW :]
    coarse_rows = coarse.size // IFW
    rows = [coarse_rows, nrhs, nrhs, nc, nc]
    at = [sum(rows[:i]) for i in range(len(rows) + 1)]
    packed = jnp.concatenate(
        [coarse.reshape(coarse_rows, IFW), first_local, last_local, first_basis, last_basis], 0)
    gathered = lax.all_gather(packed, "sub", axis=0, tiled=False)
    groups = gathered[:, : at[1]].reshape(-1, nrhs)
    level2 = jnp.dot(level2_inverse[0], groups, precision=high)
    level3_in = jnp.dot(level2_basis[0], groups, precision=high)

    is_last = position == sub - 1
    n3 = level3_inverse.shape[1]
    pick = jnp.where(is_last, level2_basis[0][:, -nc:], level2_basis[0][:, :nc])
    fold = jnp.dot(pick.T, level3_inverse, precision=high)
    edge_rows = jnp.where(is_last, level2[-nc:], level2[:nc])
    edge_local = jnp.where(is_last, last_local, first_local)
    edge_basis = jnp.where(is_last, last_basis, first_basis)
    fold_rows = nc * n3 // IFW
    cut = [fold_rows, nrhs, nc, nc]
    on = [sum(cut[:i]) for i in range(len(cut) + 1)]
    outgoing = jnp.concatenate(
        [fold.reshape(fold_rows, IFW), edge_local, edge_basis, jnp.pad(edge_rows, ((0, 0), (0, IFW - nrhs)))], 0)
    count = lax.axis_size(SPREAD)
    pairs = [(i, i + 1) for i in range(sub - 1, count - 1, sub)] + [(i + 1, i) for i in range(sub - 1, count - 1, sub)]
    incoming = lax.ppermute(outgoing, SPREAD, pairs)

    gathered_in = level3_in
    for axis in ("core", "z", "x"):
        gathered_in = lax.all_gather(gathered_in, axis, axis=0, tiled=True)
    level3 = jnp.dot(level3_inverse, gathered_in, precision=high)
    corrected = level2 + jnp.dot(level2_basis[0].T, level3, precision=high)
    own_count = coarse.shape[0] * coarse.shape[1]
    own_rows = lax.dynamic_slice_in_dim(corrected, position * own_count, own_count, 0)
    per_sub = own_rows.reshape(coarse.shape[0], coarse.shape[1], -1)
    update = local + jnp.einsum("snk,snr->srk", coarse_basis, per_sub, precision=high)

    cross_fold = incoming[: on[1]].reshape(nc, n3)
    cross_rows = incoming[on[3] : on[4], :nrhs]
    cross_coef = cross_rows + jnp.dot(cross_fold, gathered_in, precision=high)

    prev_device = lax.dynamic_index_in_dim(gathered, jnp.maximum(position - 1, 0), 0, keepdims=False)
    next_device = lax.dynamic_index_in_dim(gathered, jnp.minimum(position + 1, sub - 1), 0, keepdims=False)
    prev_rows = lax.dynamic_slice_in_dim(corrected, position * own_count - nc, nc, 0)
    next_rows = lax.dynamic_slice_in_dim(corrected, (position + 1) * own_count, nc, 0)
    first = position == 0
    cross_local = incoming[on[1] : on[2]]
    cross_basis = incoming[on[2] : on[3]]
    rim_local = jnp.stack([
        jnp.where(first, cross_local, prev_device[at[2] : at[3]]),
        jnp.where(is_last, cross_local, next_device[at[1] : at[2]])])
    rim_basis = jnp.stack([
        jnp.where(first, cross_basis, prev_device[at[4] : at[5]]),
        jnp.where(is_last, cross_basis, next_device[at[3] : at[4]])])
    rim_coef = jnp.stack([
        jnp.where(first, cross_coef, prev_rows),
        jnp.where(is_last, cross_coef, next_rows)])
    rims = rim_local + jnp.sum(rim_basis[:, :, None, :] * rim_coef[:, :, :, None], axis=1)
    from_before = rims[0:1]
    from_behind = rims[1:2]
    return add_rims(update, from_before, from_behind)


def solution(mesh):
    clus, sub = mesh.shape["clus"], mesh.shape["sub"]
    x_size = 4
    z_size = clus // (2 * x_size)
    split = Mesh(mesh.devices.reshape(x_size, z_size, 2, sub), SPREAD)
    clus_axes = ("x", "z", "core")
    in_specs = (
        P(SPREAD, None, None),
        P(SPREAD, None, None),
        P(SPREAD, None, None),
        P(clus_axes, None, None),
        P(clus_axes, None, None),
        P(clus_axes, None),
    )
    out_specs = P(SPREAD, None, None)
    return jax.shard_map(shards, mesh=split, in_specs=in_specs, out_specs=out_specs, check_vma=False)
```

```python
import jax
import jax.numpy as jnp
from jax import lax
from jax.sharding import Mesh, PartitionSpec as P

IFW = 128
SPREAD = ("x", "z", "core", "sub")


def from_behind_2(array, axis, by, only=None):
    count = lax.axis_size(axis)
    pairs = [(i, i + by) for i in range(count) if 0 <= i + by < count and (only is None or only(i))]
    return lax.ppermute(array, axis, pairs)


def couple(values_in):
    lower_rim = values_in[:, :, :IFW]
    upper_rim = values_in[:, :, values_in.shape[2] - IFW :]
    from_before = from_behind_2(upper_rim[-1:], SPREAD, 1)
    from_behind = from_behind_2(lower_rim[:1], SPREAD, -1)
    return add_rims(values_in, from_before, from_behind)


def add_rims(values_in, from_before, from_behind):
    lower_rim = values_in[:, :, :IFW]
    upper_rim = values_in[:, :, values_in.shape[2] - IFW :]
    prev_rims = jnp.concatenate([from_before, upper_rim[:-1]], 0)
    next_rims = jnp.concatenate([lower_rim[1:], from_behind], 0)
    coupled = values_in.at[:, :, :IFW].add(0.5 * prev_rims)
    return coupled.at[:, :, values_in.shape[2] - IFW :].add(0.5 * next_rims)


def rim_update(local_rim, basis_rim, coefficients):
    high = lax.Precision.HIGH
    return local_rim + jnp.einsum("snk,snr->srk", basis_rim, coefficients[None], precision=high)


def shards(residual_in, local_inverse, coarse_basis, level2_inverse, level2_basis, level3_inverse):
    high = lax.Precision.HIGH
    sub = lax.axis_size("sub")
    position = lax.axis_index("sub")
    nloc = residual_in.shape[2]
    nc = coarse_basis.shape[1]
    rhs = couple(residual_in)
    rhs_low = rhs.astype(jnp.bfloat16)
    inner = residual_in[1:-1]
    inner = inner.at[:, :, :IFW].add(0.5 * residual_in[:-2, :, nloc - IFW :])
    inner = inner.at[:, :, nloc - IFW :].add(0.5 * residual_in[2:, :, :IFW])
    inner_local = jnp.einsum(
        "srk,sjk->srj", inner.astype(jnp.bfloat16), local_inverse[1:-1], preferred_element_type=jnp.float32)
    edge_local = jnp.einsum(
        "srk,sjk->srj", rhs_low[::residual_in.shape[0] - 1], local_inverse[::residual_in.shape[0] - 1],
        preferred_element_type=jnp.float32)
    local = jnp.concatenate([edge_local[:1], inner_local, edge_local[1:]], 0)
    coarse = jnp.einsum("snk,srk->snr", coarse_basis, rhs, precision=high)
    nrhs = local.shape[1]

    first_local = local[0, :, :IFW]
    last_local = local[-1, :, nloc - IFW :]
    first_basis = coarse_basis[0, :, :IFW]
    last_basis = coarse_basis[-1, :, nloc - IFW :]
    coarse_rows = coarse.size // IFW
    rows = [coarse_rows, nrhs, nrhs, nc, nc]
    at = [sum(rows[:i]) for i in range(len(rows) + 1)]
    packed = jnp.concatenate(
        [coarse.reshape(coarse_rows, IFW), first_local, last_local, first_basis, last_basis], 0)
    gathered = lax.all_gather(packed, "sub", axis=0, tiled=False)
    groups = gathered[:, : at[1]].reshape(-1, nrhs)
    level2 = jnp.dot(level2_inverse[0], groups, precision=high)
    level3_in = jnp.dot(level2_basis[0], groups, precision=high)
    level2, level3_in = lax.optimization_barrier((level2, level3_in))

    is_last = position == sub - 1
    n3 = level3_inverse.shape[1]
    pick = jnp.where(is_last, level2_basis[0][:, -nc:], level2_basis[0][:, :nc])
    fold = jnp.dot(pick.T, level3_inverse, precision=high)
    edge_rows = jnp.where(is_last, level2[-nc:], level2[:nc])
    edge_local = jnp.where(is_last, last_local, first_local)
    edge_basis = jnp.where(is_last, last_basis, first_basis)
    fold_rows = nc * n3 // IFW
    cut = [fold_rows, nrhs, nc, nc]
    on = [sum(cut[:i]) for i in range(len(cut) + 1)]
    outgoing = jnp.concatenate(
        [fold.reshape(fold_rows, IFW), edge_local, edge_basis, jnp.pad(edge_rows, ((0, 0), (0, IFW - nrhs)))], 0)
    count = lax.axis_size(SPREAD)
    pairs = [(i, i + 1) for i in range(sub - 1, count - 1, sub)] + [(i + 1, i) for i in range(sub - 1, count - 1, sub)]
    incoming = lax.ppermute(outgoing, SPREAD, pairs)

    gathered_in = level3_in
    for axis in ("core", "z", "x"):
        gathered_in = lax.all_gather(gathered_in, axis, axis=0, tiled=True)
    incoming, gathered_in = lax.optimization_barrier((incoming, gathered_in))
    level3 = jnp.dot(level3_inverse, gathered_in, precision=high)
    corrected = level2 + jnp.dot(level2_basis[0].T, level3, precision=high)
    own_count = coarse.shape[0] * coarse.shape[1]
    own_rows = lax.dynamic_slice_in_dim(corrected, position * own_count, own_count, 0)
    per_sub = own_rows.reshape(coarse.shape[0], coarse.shape[1], -1)

    cross_fold = incoming[: on[1]].reshape(nc, n3)
    cross_rows = incoming[on[3] : on[4], :nrhs]
    cross_coef = cross_rows + jnp.dot(cross_fold, gathered_in, precision=high)

    prev_device = lax.dynamic_index_in_dim(gathered, jnp.maximum(position - 1, 0), 0, keepdims=False)
    next_device = lax.dynamic_index_in_dim(gathered, jnp.minimum(position + 1, sub - 1), 0, keepdims=False)
    prev_rows = lax.dynamic_slice_in_dim(corrected, position * own_count - nc, nc, 0)
    next_rows = lax.dynamic_slice_in_dim(corrected, (position + 1) * own_count, nc, 0)
    first = position == 0
    cross_local = incoming[on[1] : on[2]]
    cross_basis = incoming[on[2] : on[3]]
    rim_local = jnp.stack([
        jnp.where(first, cross_local, prev_device[at[2] : at[3]]),
        jnp.where(is_last, cross_local, next_device[at[1] : at[2]])])
    rim_basis = jnp.stack([
        jnp.where(first, cross_basis, prev_device[at[4] : at[5]]),
        jnp.where(is_last, cross_basis, next_device[at[3] : at[4]])])
    rim_coef = jnp.stack([
        jnp.where(first, cross_coef, prev_rows),
        jnp.where(is_last, cross_coef, next_rows)])
    rims = rim_local + jnp.sum(rim_basis[:, :, None, :] * rim_coef[:, :, :, None], axis=1)
    from_before = rims[0:1]
    from_behind = rims[1:2]
    lower = local[:, :, :IFW] + jnp.einsum("snk,snr->srk", coarse_basis[:, :, :IFW], per_sub, precision=high)
    upper = local[:, :, nloc - IFW :] + jnp.einsum(
        "snk,snr->srk", coarse_basis[:, :, nloc - IFW :], per_sub, precision=high)
    prev_rims = jnp.concatenate([from_before, upper[:-1]], 0)
    next_rims = jnp.concatenate([lower[1:], from_behind], 0)
    middle = jnp.zeros((local.shape[0], nrhs, nloc - 2 * IFW), jnp.float32)
    rim_terms = jnp.concatenate([0.5 * prev_rims, middle, 0.5 * next_rims], 2)
    update = local + jnp.einsum("snk,snr->srk", coarse_basis, per_sub, precision=high)
    return update + rim_terms


def solution(mesh):
    clus, sub = mesh.shape["clus"], mesh.shape["sub"]
    x_size = 4
    z_size = clus // (2 * x_size)
    split = Mesh(mesh.devices.reshape(x_size, z_size, 2, sub), SPREAD)
    clus_axes = ("x", "z", "core")
    in_specs = (
        P(SPREAD, None, None),
        P(SPREAD, None, None),
        P(SPREAD, None, None),
        P(clus_axes, None, None),
        P(clus_axes, None, None),
        P(clus_axes, None),
    )
    out_specs = P(SPREAD, None, None)
    return jax.shard_map(shards, mesh=split, in_specs=in_specs, out_specs=out_specs, check_vma=False)
```

```python
import jax
import jax.numpy as jnp
from jax import lax
from jax.sharding import Mesh, PartitionSpec as P

IFW = 128
SPREAD = ("x", "z", "core", "sub")


def from_behind_2(array, axis, by, only=None):
    count = lax.axis_size(axis)
    pairs = [(i, i + by) for i in range(count) if 0 <= i + by < count and (only is None or only(i))]
    return lax.ppermute(array, axis, pairs)


def couple(values_in):
    lower_rim = values_in[:, :, :IFW]
    upper_rim = values_in[:, :, values_in.shape[2] - IFW :]
    from_before = from_behind_2(upper_rim[-1:], SPREAD, 1)
    from_behind = from_behind_2(lower_rim[:1], SPREAD, -1)
    return add_rims(values_in, from_before, from_behind)


def add_rims(values_in, from_before, from_behind):
    lower_rim = values_in[:, :, :IFW]
    upper_rim = values_in[:, :, values_in.shape[2] - IFW :]
    prev_rims = jnp.concatenate([from_before, upper_rim[:-1]], 0)
    next_rims = jnp.concatenate([lower_rim[1:], from_behind], 0)
    coupled = values_in.at[:, :, :IFW].add(0.5 * prev_rims)
    return coupled.at[:, :, values_in.shape[2] - IFW :].add(0.5 * next_rims)


def rim_update(local_rim, basis_rim, coefficients):
    high = lax.Precision.HIGH
    return local_rim + jnp.einsum("snk,snr->srk", basis_rim, coefficients[None], precision=high)


def shards(residual_in, local_inverse, coarse_basis, level2_inverse, level2_basis, level3_inverse):
    high = lax.Precision.HIGH
    sub = lax.axis_size("sub")
    position = lax.axis_index("sub")
    nloc = residual_in.shape[2]
    nc = coarse_basis.shape[1]
    rhs = couple(residual_in)
    rhs_low = rhs.astype(jnp.bfloat16)
    inner = residual_in[1:-1]
    inner = inner.at[:, :, :IFW].add(0.5 * residual_in[:-2, :, nloc - IFW :])
    inner = inner.at[:, :, nloc - IFW :].add(0.5 * residual_in[2:, :, :IFW])
    inner_local = jnp.einsum(
        "srk,sjk->srj", inner.astype(jnp.bfloat16), local_inverse[1:-1], preferred_element_type=jnp.float32)
    edge_local = jnp.einsum(
        "srk,sjk->srj", rhs_low[::residual_in.shape[0] - 1], local_inverse[::residual_in.shape[0] - 1],
        preferred_element_type=jnp.float32)
    local = jnp.concatenate([edge_local[:1], inner_local, edge_local[1:]], 0)
    coarse = jnp.einsum("snk,srk->snr", coarse_basis, rhs, precision=high)
    nrhs = local.shape[1]

    first_local = local[0, :, :IFW]
    last_local = local[-1, :, nloc - IFW :]
    first_basis = coarse_basis[0, :, :IFW]
    last_basis = coarse_basis[-1, :, nloc - IFW :]
    coarse_rows = coarse.size // IFW
    rows = [coarse_rows, nrhs, nrhs, nc, nc]
    at = [sum(rows[:i]) for i in range(len(rows) + 1)]
    packed = jnp.concatenate(
        [coarse.reshape(coarse_rows, IFW), first_local, last_local, first_basis, last_basis], 0)
    gathered = lax.all_gather(packed, "sub", axis=0, tiled=False)
    groups = gathered[:, : at[1]].reshape(-1, nrhs)
    level2 = jnp.dot(level2_inverse[0], groups, precision=high)
    level3_in = jnp.dot(level2_basis[0], groups, precision=high)

    is_last = position == sub - 1
    n3 = level3_inverse.shape[1]
    pick = jnp.where(is_last, level2_basis[0][:, -nc:], level2_basis[0][:, :nc])
    fold = jnp.dot(pick.T, level3_inverse, precision=high)
    edge_rows = jnp.where(is_last, level2[-nc:], level2[:nc])
    edge_local = jnp.where(is_last, last_local, first_local)
    edge_basis = jnp.where(is_last, last_basis, first_basis)
    fold_rows = nc * n3 // IFW
    cut = [fold_rows, nrhs, nc, nc]
    on = [sum(cut[:i]) for i in range(len(cut) + 1)]
    outgoing = jnp.concatenate(
        [fold.reshape(fold_rows, IFW), edge_local, edge_basis, jnp.pad(edge_rows, ((0, 0), (0, IFW - nrhs)))], 0)
    count = lax.axis_size(SPREAD)
    pairs = [(i, i + 1) for i in range(sub - 1, count - 1, sub)] + [(i + 1, i) for i in range(sub - 1, count - 1, sub)]
    incoming = lax.ppermute(outgoing, SPREAD, pairs)

    gathered_in = level3_in
    for axis in ("core", "z", "x"):
        gathered_in = lax.all_gather(gathered_in, axis, axis=0, tiled=True)
    level3 = jnp.dot(level3_inverse, gathered_in, precision=high)
    corrected = level2 + jnp.dot(level2_basis[0].T, level3, precision=high)
    own_count = coarse.shape[0] * coarse.shape[1]
    own_rows = lax.dynamic_slice_in_dim(corrected, position * own_count, own_count, 0)
    per_sub = own_rows.reshape(coarse.shape[0], coarse.shape[1], -1)
    update = local + jnp.einsum("snk,snr->srk", coarse_basis, per_sub, precision=high)

    cross_fold = incoming[: on[1]].reshape(nc, n3)
    cross_rows = incoming[on[3] : on[4], :nrhs]
    cross_coef = cross_rows + jnp.dot(cross_fold, gathered_in, precision=high)

    prev_device = lax.dynamic_index_in_dim(gathered, jnp.maximum(position - 1, 0), 0, keepdims=False)
    next_device = lax.dynamic_index_in_dim(gathered, jnp.minimum(position + 1, sub - 1), 0, keepdims=False)
    prev_rows = lax.dynamic_slice_in_dim(corrected, position * own_count - nc, nc, 0)
    next_rows = lax.dynamic_slice_in_dim(corrected, (position + 1) * own_count, nc, 0)
    first = position == 0
    cross_local = incoming[on[1] : on[2]]
    cross_basis = incoming[on[2] : on[3]]
    rim_local = jnp.stack([
        jnp.where(first, cross_local, prev_device[at[2] : at[3]]),
        jnp.where(is_last, cross_local, next_device[at[1] : at[2]])])
    rim_basis = jnp.stack([
        jnp.where(first, cross_basis, prev_device[at[4] : at[5]]),
        jnp.where(is_last, cross_basis, next_device[at[3] : at[4]])])
    rim_coef = jnp.stack([
        jnp.where(first, cross_coef, prev_rows),
        jnp.where(is_last, cross_coef, next_rows)])
    rims = rim_local + jnp.sum(rim_basis[:, :, None, :] * rim_coef[:, :, :, None], axis=1)
    from_before = rims[0:1]
    from_behind = rims[1:2]
    lower_rim = update[:, :, :IFW]
    upper_rim = update[:, :, nloc - IFW :]
    new_lower = lower_rim + 0.5 * jnp.concatenate([from_before, upper_rim[:-1]], 0)
    new_upper = upper_rim + 0.5 * jnp.concatenate([lower_rim[1:], from_behind], 0)
    return jnp.concatenate([new_lower, update[:, :, IFW : nloc - IFW], new_upper], 2)


def solution(mesh):
    clus, sub = mesh.shape["clus"], mesh.shape["sub"]
    x_size = 4
    z_size = clus // (2 * x_size)
    split = Mesh(mesh.devices.reshape(x_size, z_size, 2, sub), SPREAD)
    clus_axes = ("x", "z", "core")
    in_specs = (
        P(SPREAD, None, None),
        P(SPREAD, None, None),
        P(SPREAD, None, None),
        P(clus_axes, None, None),
        P(clus_axes, None, None),
        P(clus_axes, None),
    )
    out_specs = P(SPREAD, None, None)
    return jax.shard_map(shards, mesh=split, in_specs=in_specs, out_specs=out_specs, check_vma=False)
```

```python
import jax
import jax.numpy as jnp
from jax import lax
from jax.sharding import Mesh, PartitionSpec as P

IFW = 128
SPREAD = ("x", "z", "core", "sub")


def from_behind_2(array, axis, by, only=None):
    count = lax.axis_size(axis)
    pairs = [(i, i + by) for i in range(count) if 0 <= i + by < count and (only is None or only(i))]
    return lax.ppermute(array, axis, pairs)


def couple(values_in):
    lower_rim = values_in[:, :, :IFW]
    upper_rim = values_in[:, :, values_in.shape[2] - IFW :]
    from_before = from_behind_2(upper_rim[-1:], SPREAD, 1)
    from_behind = from_behind_2(lower_rim[:1], SPREAD, -1)
    return add_rims(values_in, from_before, from_behind)


def add_rims(values_in, from_before, from_behind):
    lower_rim = values_in[:, :, :IFW]
    upper_rim = values_in[:, :, values_in.shape[2] - IFW :]
    prev_rims = jnp.concatenate([from_before, upper_rim[:-1]], 0)
    next_rims = jnp.concatenate([lower_rim[1:], from_behind], 0)
    coupled = values_in.at[:, :, :IFW].add(0.5 * prev_rims)
    return coupled.at[:, :, values_in.shape[2] - IFW :].add(0.5 * next_rims)


def rim_update(local_rim, basis_rim, coefficients):
    high = lax.Precision.HIGH
    return local_rim + jnp.einsum("snk,snr->srk", basis_rim, coefficients[None], precision=high)


def shards(residual_in, local_inverse, coarse_basis, level2_inverse, level2_basis, level3_inverse):
    high = lax.Precision.HIGH
    sub = lax.axis_size("sub")
    position = lax.axis_index("sub")
    nloc = residual_in.shape[2]
    nc = coarse_basis.shape[1]
    rhs = couple(residual_in)
    rhs_low = rhs.astype(jnp.bfloat16)
    inner = residual_in[1:-1]
    inner = inner.at[:, :, :IFW].add(0.5 * residual_in[:-2, :, nloc - IFW :])
    inner = inner.at[:, :, nloc - IFW :].add(0.5 * residual_in[2:, :, :IFW])
    inner_local = jnp.einsum(
        "srk,sjk->srj", inner.astype(jnp.bfloat16), local_inverse[1:-1], preferred_element_type=jnp.float32)
    edge_local = jnp.einsum(
        "srk,sjk->srj", rhs_low[::residual_in.shape[0] - 1], local_inverse[::residual_in.shape[0] - 1],
        preferred_element_type=jnp.float32)
    local = jnp.concatenate([edge_local[:1], inner_local, edge_local[1:]], 0)
    coarse = jnp.einsum("snk,srk->snr", coarse_basis, rhs, precision=high)
    nrhs = local.shape[1]

    first_local = local[0, :, :IFW]
    last_local = local[-1, :, nloc - IFW :]
    first_basis = coarse_basis[0, :, :IFW]
    last_basis = coarse_basis[-1, :, nloc - IFW :]
    coarse_rows = coarse.size // IFW
    rows = [coarse_rows, nrhs, nrhs, nc, nc]
    at = [sum(rows[:i]) for i in range(len(rows) + 1)]
    packed = jnp.concatenate(
        [coarse.reshape(coarse_rows, IFW), first_local, last_local, first_basis, last_basis], 0)
    gathered = lax.all_gather(packed, "sub", axis=0, tiled=False)
    groups = gathered[:, : at[1]].reshape(-1, nrhs)
    level2 = jnp.dot(level2_inverse[0], groups, precision=high)
    level3_in = jnp.dot(level2_basis[0], groups, precision=high)

    is_last = position == sub - 1
    n3 = level3_inverse.shape[1]
    pick = jnp.where(is_last, level2_basis[0][:, -nc:], level2_basis[0][:, :nc])
    fold = jnp.dot(pick.T, level3_inverse, precision=high)
    edge_rows = jnp.where(is_last, level2[-nc:], level2[:nc])
    edge_local = jnp.where(is_last, last_local, first_local)
    edge_basis = jnp.where(is_last, last_basis, first_basis)
    fold_rows = nc * n3 // IFW
    cut = [fold_rows, nrhs, nc, nc]
    on = [sum(cut[:i]) for i in range(len(cut) + 1)]
    outgoing = jnp.concatenate(
        [fold.reshape(fold_rows, IFW), edge_local, edge_basis, jnp.pad(edge_rows, ((0, 0), (0, IFW - nrhs)))], 0)
    count = lax.axis_size(SPREAD)
    pairs = [(i, i + 1) for i in range(sub - 1, count - 1, sub)] + [(i + 1, i) for i in range(sub - 1, count - 1, sub)]
    gathered_in = level3_in
    for axis in ("core", "z"):
        gathered_in = lax.all_gather(gathered_in, axis, axis=0, tiled=True)
    outgoing, gathered_in = lax.optimization_barrier((outgoing, gathered_in))
    incoming = lax.ppermute(outgoing, SPREAD, pairs)
    gathered_in = lax.all_gather(gathered_in, "x", axis=0, tiled=True)
    level3 = jnp.dot(level3_inverse, gathered_in, precision=high)
    corrected = level2 + jnp.dot(level2_basis[0].T, level3, precision=high)
    own_count = coarse.shape[0] * coarse.shape[1]
    own_rows = lax.dynamic_slice_in_dim(corrected, position * own_count, own_count, 0)
    per_sub = own_rows.reshape(coarse.shape[0], coarse.shape[1], -1)
    update = local + jnp.einsum("snk,snr->srk", coarse_basis, per_sub, precision=high)

    cross_fold = incoming[: on[1]].reshape(nc, n3)
    cross_rows = incoming[on[3] : on[4], :nrhs]
    cross_coef = cross_rows + jnp.dot(cross_fold, gathered_in, precision=high)

    prev_device = lax.dynamic_index_in_dim(gathered, jnp.maximum(position - 1, 0), 0, keepdims=False)
    next_device = lax.dynamic_index_in_dim(gathered, jnp.minimum(position + 1, sub - 1), 0, keepdims=False)
    prev_rows = lax.dynamic_slice_in_dim(corrected, position * own_count - nc, nc, 0)
    next_rows = lax.dynamic_slice_in_dim(corrected, (position + 1) * own_count, nc, 0)
    first = position == 0
    cross_local = incoming[on[1] : on[2]]
    cross_basis = incoming[on[2] : on[3]]
    rim_local = jnp.stack([
        jnp.where(first, cross_local, prev_device[at[2] : at[3]]),
        jnp.where(is_last, cross_local, next_device[at[1] : at[2]])])
    rim_basis = jnp.stack([
        jnp.where(first, cross_basis, prev_device[at[4] : at[5]]),
        jnp.where(is_last, cross_basis, next_device[at[3] : at[4]])])
    rim_coef = jnp.stack([
        jnp.where(first, cross_coef, prev_rows),
        jnp.where(is_last, cross_coef, next_rows)])
    rims = rim_local + jnp.sum(rim_basis[:, :, None, :] * rim_coef[:, :, :, None], axis=1)
    from_before = rims[0:1]
    from_behind = rims[1:2]
    lower_rim = update[:, :, :IFW]
    upper_rim = update[:, :, nloc - IFW :]
    new_lower = lower_rim + 0.5 * jnp.concatenate([from_before, upper_rim[:-1]], 0)
    new_upper = upper_rim + 0.5 * jnp.concatenate([lower_rim[1:], from_behind], 0)
    return jnp.concatenate([new_lower, update[:, :, IFW : nloc - IFW], new_upper], 2)


def solution(mesh):
    clus, sub = mesh.shape["clus"], mesh.shape["sub"]
    x_size = 4
    z_size = clus // (2 * x_size)
    split = Mesh(mesh.devices.reshape(x_size, z_size, 2, sub), SPREAD)
    clus_axes = ("x", "z", "core")
    in_specs = (
        P(SPREAD, None, None),
        P(SPREAD, None, None),
        P(SPREAD, None, None),
        P(clus_axes, None, None),
        P(clus_axes, None, None),
        P(clus_axes, None),
    )
    out_specs = P(SPREAD, None, None)
    return jax.shard_map(shards, mesh=split, in_specs=in_specs, out_specs=out_specs, check_vma=False)
```

```python
import jax
import jax.numpy as jnp
from jax import lax
from jax.sharding import Mesh, PartitionSpec as P

IFW = 128
SPREAD = ("x", "z", "core", "sub")


def from_behind_2(array, axis, by, only=None):
    count = lax.axis_size(axis)
    pairs = [(i, i + by) for i in range(count) if 0 <= i + by < count and (only is None or only(i))]
    return lax.ppermute(array, axis, pairs)


def couple(values_in):
    lower_rim = values_in[:, :, :IFW]
    upper_rim = values_in[:, :, values_in.shape[2] - IFW :]
    from_before = from_behind_2(upper_rim[-1:], SPREAD, 1)
    from_behind = from_behind_2(lower_rim[:1], SPREAD, -1)
    return add_rims(values_in, from_before, from_behind)


def add_rims(values_in, from_before, from_behind):
    lower_rim = values_in[:, :, :IFW]
    upper_rim = values_in[:, :, values_in.shape[2] - IFW :]
    prev_rims = jnp.concatenate([from_before, upper_rim[:-1]], 0)
    next_rims = jnp.concatenate([lower_rim[1:], from_behind], 0)
    coupled = values_in.at[:, :, :IFW].add(0.5 * prev_rims)
    return coupled.at[:, :, values_in.shape[2] - IFW :].add(0.5 * next_rims)


def rim_update(local_rim, basis_rim, coefficients):
    high = lax.Precision.HIGH
    return local_rim + jnp.einsum("snk,snr->srk", basis_rim, coefficients[None], precision=high)


def shards(residual_in, local_inverse, coarse_basis, level2_inverse, level2_basis, level3_inverse):
    high = lax.Precision.HIGH
    sub = lax.axis_size("sub")
    position = lax.axis_index("sub")
    nloc = residual_in.shape[2]
    nc = coarse_basis.shape[1]
    rhs = couple(residual_in)
    rhs_low = rhs.astype(jnp.bfloat16)
    inner = residual_in[1:-1]
    inner = inner.at[:, :, :IFW].add(0.5 * residual_in[:-2, :, nloc - IFW :])
    inner = inner.at[:, :, nloc - IFW :].add(0.5 * residual_in[2:, :, :IFW])
    inner_local = jnp.einsum(
        "srk,sjk->srj", inner.astype(jnp.bfloat16), local_inverse[1:-1], preferred_element_type=jnp.float32)
    edge_local = jnp.einsum(
        "srk,sjk->srj", rhs_low[::residual_in.shape[0] - 1], local_inverse[::residual_in.shape[0] - 1],
        preferred_element_type=jnp.float32)
    local = jnp.concatenate([edge_local[:1], inner_local, edge_local[1:]], 0)
    coarse = jnp.einsum("snk,srk->snr", coarse_basis, rhs, precision=high)
    nrhs = local.shape[1]

    first_local = local[0, :, :IFW]
    last_local = local[-1, :, nloc - IFW :]
    first_basis = coarse_basis[0, :, :IFW]
    last_basis = coarse_basis[-1, :, nloc - IFW :]
    coarse_rows = coarse.size // IFW
    rows = [coarse_rows, nrhs, nrhs, nc, nc]
    at = [sum(rows[:i]) for i in range(len(rows) + 1)]
    packed = jnp.concatenate(
        [coarse.reshape(coarse_rows, IFW), first_local, last_local, first_basis, last_basis], 0)
    gathered = lax.all_gather(packed, "sub", axis=0, tiled=False)
    groups = gathered[:, : at[1]].reshape(-1, nrhs)
    level2 = jnp.dot(level2_inverse[0], groups, precision=high)
    level3_in = jnp.dot(level2_basis[0], groups, precision=high)

    is_last = position == sub - 1
    n3 = level3_inverse.shape[1]
    pick = jnp.where(is_last, level2_basis[0][:, -nc:], level2_basis[0][:, :nc])
    fold = jnp.dot(pick.T, level3_inverse, precision=high)
    edge_rows = jnp.where(is_last, level2[-nc:], level2[:nc])
    edge_local = jnp.where(is_last, last_local, first_local)
    edge_basis = jnp.where(is_last, last_basis, first_basis)
    fold_rows = nc * n3 // IFW
    cut = [fold_rows, nrhs, nc, nc]
    on = [sum(cut[:i]) for i in range(len(cut) + 1)]
    outgoing = jnp.concatenate(
        [fold.reshape(fold_rows, IFW), edge_local, edge_basis, jnp.pad(edge_rows, ((0, 0), (0, IFW - nrhs)))], 0)
    count = lax.axis_size(SPREAD)
    pairs = [(i, i + 1) for i in range(sub - 1, count - 1, sub)] + [(i + 1, i) for i in range(sub - 1, count - 1, sub)]
    gathered_in = level3_in.reshape(-1, IFW)
    for axis in ("core", "z"):
        gathered_in = lax.all_gather(gathered_in, axis, axis=0, tiled=True)
    outgoing, gathered_in = lax.optimization_barrier((outgoing, gathered_in))
    incoming = lax.ppermute(outgoing, SPREAD, pairs)
    gathered_in = lax.all_gather(gathered_in, "x", axis=0, tiled=True).reshape(-1, nrhs)
    level3 = jnp.dot(level3_inverse, gathered_in, precision=high)
    corrected = level2 + jnp.dot(level2_basis[0].T, level3, precision=high)
    own_count = coarse.shape[0] * coarse.shape[1]
    own_rows = lax.dynamic_slice_in_dim(corrected, position * own_count, own_count, 0)
    per_sub = own_rows.reshape(coarse.shape[0], coarse.shape[1], -1)
    update = local + jnp.einsum("snk,snr->srk", coarse_basis, per_sub, precision=high)

    cross_fold = incoming[: on[1]].reshape(nc, n3)
    cross_rows = incoming[on[3] : on[4], :nrhs]
    cross_coef = cross_rows + jnp.dot(cross_fold, gathered_in, precision=high)

    prev_device = lax.dynamic_index_in_dim(gathered, jnp.maximum(position - 1, 0), 0, keepdims=False)
    next_device = lax.dynamic_index_in_dim(gathered, jnp.minimum(position + 1, sub - 1), 0, keepdims=False)
    prev_rows = lax.dynamic_slice_in_dim(corrected, position * own_count - nc, nc, 0)
    next_rows = lax.dynamic_slice_in_dim(corrected, (position + 1) * own_count, nc, 0)
    first = position == 0
    cross_local = incoming[on[1] : on[2]]
    cross_basis = incoming[on[2] : on[3]]
    rim_local = jnp.stack([
        jnp.where(first, cross_local, prev_device[at[2] : at[3]]),
        jnp.where(is_last, cross_local, next_device[at[1] : at[2]])])
    rim_basis = jnp.stack([
        jnp.where(first, cross_basis, prev_device[at[4] : at[5]]),
        jnp.where(is_last, cross_basis, next_device[at[3] : at[4]])])
    rim_coef = jnp.stack([
        jnp.where(first, cross_coef, prev_rows),
        jnp.where(is_last, cross_coef, next_rows)])
    rims = rim_local + jnp.sum(rim_basis[:, :, None, :] * rim_coef[:, :, :, None], axis=1)
    from_before = rims[0:1]
    from_behind = rims[1:2]
    lower_rim = update[:, :, :IFW]
    upper_rim = update[:, :, nloc - IFW :]
    new_lower = lower_rim + 0.5 * jnp.concatenate([from_before, upper_rim[:-1]], 0)
    new_upper = upper_rim + 0.5 * jnp.concatenate([lower_rim[1:], from_behind], 0)
    return jnp.concatenate([new_lower, update[:, :, IFW : nloc - IFW], new_upper], 2)


def solution(mesh):
    clus, sub = mesh.shape["clus"], mesh.shape["sub"]
    x_size = 4
    z_size = clus // (2 * x_size)
    split = Mesh(mesh.devices.reshape(x_size, z_size, 2, sub), SPREAD)
    clus_axes = ("x", "z", "core")
    in_specs = (
        P(SPREAD, None, None),
        P(SPREAD, None, None),
        P(SPREAD, None, None),
        P(clus_axes, None, None),
        P(clus_axes, None, None),
        P(clus_axes, None),
    )
    out_specs = P(SPREAD, None, None)
    return jax.shard_map(shards, mesh=split, in_specs=in_specs, out_specs=out_specs, check_vma=False)
```

```python
import jax
import jax.numpy as jnp
from jax import lax
from jax.sharding import Mesh, PartitionSpec as P

IFW = 128
SPREAD = ("x", "z", "core", "sub")


def from_behind_2(array, axis, by, only=None):
    count = lax.axis_size(axis)
    pairs = [(i, i + by) for i in range(count) if 0 <= i + by < count and (only is None or only(i))]
    return lax.ppermute(array, axis, pairs)


def couple(values_in):
    lower_rim = values_in[:, :, :IFW]
    upper_rim = values_in[:, :, values_in.shape[2] - IFW :]
    from_before = from_behind_2(upper_rim[-1:], SPREAD, 1)
    from_behind = from_behind_2(lower_rim[:1], SPREAD, -1)
    return add_rims(values_in, from_before, from_behind)


def add_rims(values_in, from_before, from_behind):
    lower_rim = values_in[:, :, :IFW]
    upper_rim = values_in[:, :, values_in.shape[2] - IFW :]
    prev_rims = jnp.concatenate([from_before, upper_rim[:-1]], 0)
    next_rims = jnp.concatenate([lower_rim[1:], from_behind], 0)
    coupled = values_in.at[:, :, :IFW].add(0.5 * prev_rims)
    return coupled.at[:, :, values_in.shape[2] - IFW :].add(0.5 * next_rims)


def rim_update(local_rim, basis_rim, coefficients):
    high = lax.Precision.HIGH
    return local_rim + jnp.einsum("snk,snr->srk", basis_rim, coefficients[None], precision=high)


def shards(residual_in, local_inverse, coarse_basis, level2_inverse, level2_basis, level3_inverse):
    high = lax.Precision.HIGH
    sub = lax.axis_size("sub")
    position = lax.axis_index("sub")
    nloc = residual_in.shape[2]
    nc = coarse_basis.shape[1]
    rhs = couple(residual_in)
    rhs_low = rhs.astype(jnp.bfloat16)
    inner = residual_in[1:-1]
    inner = inner.at[:, :, :IFW].add(0.5 * residual_in[:-2, :, nloc - IFW :])
    inner = inner.at[:, :, nloc - IFW :].add(0.5 * residual_in[2:, :, :IFW])
    inner_local = jnp.einsum(
        "srk,sjk->srj", inner.astype(jnp.bfloat16), local_inverse[1:-1], preferred_element_type=jnp.float32)
    edge_local = jnp.einsum(
        "srk,sjk->srj", rhs_low[::residual_in.shape[0] - 1], local_inverse[::residual_in.shape[0] - 1],
        preferred_element_type=jnp.float32)
    local = jnp.concatenate([edge_local[:1], inner_local, edge_local[1:]], 0)
    inner_coarse = jnp.einsum("snk,srk->snr", coarse_basis[1:-1], inner, precision=high)
    edge_coarse = jnp.einsum(
        "snk,srk->snr", coarse_basis[::residual_in.shape[0] - 1], rhs[::residual_in.shape[0] - 1], precision=high)
    coarse = jnp.concatenate([edge_coarse[:1], inner_coarse, edge_coarse[1:]], 0)
    nrhs = local.shape[1]

    first_local = local[0, :, :IFW]
    last_local = local[-1, :, nloc - IFW :]
    first_basis = coarse_basis[0, :, :IFW]
    last_basis = coarse_basis[-1, :, nloc - IFW :]
    coarse_rows = coarse.size // IFW
    rows = [coarse_rows, nrhs, nrhs, nc, nc]
    at = [sum(rows[:i]) for i in range(len(rows) + 1)]
    packed = jnp.concatenate(
        [coarse.reshape(coarse_rows, IFW), first_local, last_local, first_basis, last_basis], 0)
    gathered = lax.all_gather(packed, "sub", axis=0, tiled=False)
    groups = gathered[:, : at[1]].reshape(-1, nrhs)
    level2 = jnp.dot(level2_inverse[0], groups, precision=high)
    level3_in = jnp.dot(level2_basis[0], groups, precision=high)

    is_last = position == sub - 1
    n3 = level3_inverse.shape[1]
    pick = jnp.where(is_last, level2_basis[0][:, -nc:], level2_basis[0][:, :nc])
    fold = jnp.dot(pick.T, level3_inverse, precision=high)
    edge_rows = jnp.where(is_last, level2[-nc:], level2[:nc])
    edge_local = jnp.where(is_last, last_local, first_local)
    edge_basis = jnp.where(is_last, last_basis, first_basis)
    fold_rows = nc * n3 // IFW
    cut = [fold_rows, nrhs, nc, nc]
    on = [sum(cut[:i]) for i in range(len(cut) + 1)]
    outgoing = jnp.concatenate(
        [fold.reshape(fold_rows, IFW), edge_local, edge_basis, jnp.pad(edge_rows, ((0, 0), (0, IFW - nrhs)))], 0)
    count = lax.axis_size(SPREAD)
    pairs = [(i, i + 1) for i in range(sub - 1, count - 1, sub)] + [(i + 1, i) for i in range(sub - 1, count - 1, sub)]
    gathered_in = level3_in
    for axis in ("core", "z"):
        gathered_in = lax.all_gather(gathered_in, axis, axis=0, tiled=True)
    outgoing, gathered_in = lax.optimization_barrier((outgoing, gathered_in))
    incoming = lax.ppermute(outgoing, SPREAD, pairs)
    gathered_in = lax.all_gather(gathered_in, "x", axis=0, tiled=True)
    level3 = jnp.dot(level3_inverse, gathered_in, precision=high)
    corrected = level2 + jnp.dot(level2_basis[0].T, level3, precision=high)
    own_count = coarse.shape[0] * coarse.shape[1]
    own_rows = lax.dynamic_slice_in_dim(corrected, position * own_count, own_count, 0)
    per_sub = own_rows.reshape(coarse.shape[0], coarse.shape[1], -1)
    update = local + jnp.einsum("snk,snr->srk", coarse_basis, per_sub, precision=high)

    cross_fold = incoming[: on[1]].reshape(nc, n3)
    cross_rows = incoming[on[3] : on[4], :nrhs]
    cross_coef = cross_rows + jnp.dot(cross_fold, gathered_in, precision=high)

    prev_device = lax.dynamic_index_in_dim(gathered, jnp.maximum(position - 1, 0), 0, keepdims=False)
    next_device = lax.dynamic_index_in_dim(gathered, jnp.minimum(position + 1, sub - 1), 0, keepdims=False)
    prev_rows = lax.dynamic_slice_in_dim(corrected, position * own_count - nc, nc, 0)
    next_rows = lax.dynamic_slice_in_dim(corrected, (position + 1) * own_count, nc, 0)
    first = position == 0
    cross_local = incoming[on[1] : on[2]]
    cross_basis = incoming[on[2] : on[3]]
    rim_local = jnp.stack([
        jnp.where(first, cross_local, prev_device[at[2] : at[3]]),
        jnp.where(is_last, cross_local, next_device[at[1] : at[2]])])
    rim_basis = jnp.stack([
        jnp.where(first, cross_basis, prev_device[at[4] : at[5]]),
        jnp.where(is_last, cross_basis, next_device[at[3] : at[4]])])
    rim_coef = jnp.stack([
        jnp.where(first, cross_coef, prev_rows),
        jnp.where(is_last, cross_coef, next_rows)])
    rims = rim_local + jnp.sum(rim_basis[:, :, None, :] * rim_coef[:, :, :, None], axis=1)
    from_before = rims[0:1]
    from_behind = rims[1:2]
    lower_rim = update[:, :, :IFW]
    upper_rim = update[:, :, nloc - IFW :]
    new_lower = lower_rim + 0.5 * jnp.concatenate([from_before, upper_rim[:-1]], 0)
    new_upper = upper_rim + 0.5 * jnp.concatenate([lower_rim[1:], from_behind], 0)
    return jnp.concatenate([new_lower, update[:, :, IFW : nloc - IFW], new_upper], 2)


def solution(mesh):
    clus, sub = mesh.shape["clus"], mesh.shape["sub"]
    x_size = 4
    z_size = clus // (2 * x_size)
    split = Mesh(mesh.devices.reshape(x_size, z_size, 2, sub), SPREAD)
    clus_axes = ("x", "z", "core")
    in_specs = (
        P(SPREAD, None, None),
        P(SPREAD, None, None),
        P(SPREAD, None, None),
        P(clus_axes, None, None),
        P(clus_axes, None, None),
        P(clus_axes, None),
    )
    out_specs = P(SPREAD, None, None)
    return jax.shard_map(shards, mesh=split, in_specs=in_specs, out_specs=out_specs, check_vma=False)
```
